256 devices in a mesh: seq: 32 (over x, z_lo, core), mp: 8 (over y, z_hi).
Axes of the slice: x: 4, y: 4, z: 8 (z_hi: 2, z_lo: 4; z = z_hi * 4 + z_lo), core: 2. Of those that a mesh axis runs over, the one named last changes fastest.
Arguments:
- tokens: bfloat16 [8192, 4096], P('seq', 'mp'), may hold values from -6 to 6
- norm_gain: bfloat16 [4096], replicated, may hold values from 0.5 to 1.5
- norm_bias: bfloat16 [4096], replicated, may hold values from -4 to 4
- w_query: bfloat16 [4096, 2048], P(None, 'mp'), may hold values from -0.25 to 0.25
- w_keyval: bfloat16 [4096, 2, 2048], P(None, None, 'mp'), may hold values from -0.09375 to 0.09375
- w_out: bfloat16 [2048, 4096], P('mp'), may hold values from -0.125 to 0.125
- prefix_key: bfloat16 [8192, 2048], P('seq', 'mp'), may hold values from -82 to 82
- prefix_value: bfloat16 [8192, 2048], P('seq', 'mp'), may hold values from -6 to 6
- lengths: int32 [16], replicated, may hold values from 1 to 1024, 8192 in all
- context: int32 [16], replicated, may hold values from 256 to 8192
- prefix_place: int32 [64], replicated, may hold values from 0 to 63, each once
Outputs:
- attn_out: bfloat16 [8192, 4096], P(('seq', 'mp'))
The draws below stay inside these ranges and needn't reach their ends.
Inputs may be any that keep to these rules, and one draw needn't show every extreme that they name: The lengths add up to 8192, and one request has exactly 1024 tokens. Stored block j holds the prefix positions prefix_place[j] * 128 to prefix_place[j] * 128 + 127; every block appears once.
All inputs are finite; a program needn't handle non-finite values.
Results may differ from the reference program's by a relative error of at most 0.02.
The reference program's roundings to bfloat16 on the way count: a program that leaves them out, or rounds other values in their place, can miss the bound.
Values may be sent and summed in bfloat16 or wider, within the bound.
No kernel may reach another device: no remote copies, remote signals or barrier semaphores. Data moves between devices by JAX's collectives and lax.ppermute only.
A program may use at most 128 MiB of HBM per device.

```python
import math
import jax
import jax.numpy as jnp
import numpy as np
from jax import lax

D = 4096
HEADS = 16
HD = 128
PBLOCK = 128
TOKENS = 8192
PREFIX = 8192
PBLOCKS = 64
REQS = 16
MOST = 1024


def draw_prefix_key(key, part):
    base_key = jax.random.fold_in(jax.random.fold_in(key, 11), 0)
    columns = HEADS * HD
    return jnp.clip(jax.random.normal(base_key, (PREFIX, columns), jnp.float32), -6.0, 6.0).astype(jnp.bfloat16)


def plant(array, rng, smallest, high):
    index_at = [jax.random.randint(jax.random.fold_in(rng, axis), (), 0, length) for axis, length in enumerate(array.shape)]
    main_axis = array.shape.index(max(array.shape))
    next_to = index_at[:main_axis] + [(index_at[main_axis] + 1) % array.shape[main_axis]] + index_at[main_axis + 1:]
    return array.at[tuple(index_at)].set(smallest).at[tuple(next_to)].set(high)


def block_scale(stream_key, dims, cuts, smallest, largest):
    loudness, own = 1.0, jax.random.fold_in(stream_key, 6)
    for dim, shards_of in cuts:
        steps = jnp.exp(jax.random.uniform(jax.random.fold_in(own, dim), (shards_of,), jnp.float32, smallest / len(cuts), largest / len(cuts)))
        loudness = loudness * jnp.repeat(steps, dims[dim] // shards_of).reshape([-1 if axis == dim else 1 for axis in range(len(dims))])
    return loudness


def split_up(number_of, total, bound, skew):
    portions = [(1 << 20) // math.isqrt(grade ** skew) + 1 for grade in range(2, number_of + 1)]
    rest, holding = total - bound - (number_of - 1), [1] * (number_of - 1)
    while rest > 0:
        free = [i for i in range(number_of - 1) if holding[i] < bound]
        mass, remaining = sum([portions[i] for i in free]), rest
        for i in free:
            extra = min(bound - holding[i], max(1, remaining * portions[i] // mass), rest)
            holding[i] = holding[i] + extra
            rest = rest - extra
    return np.array([bound] + holding)


def uneven_parts(rng, amount, total, limit, skew):
    if amount == 2:
        one = jax.random.randint(rng, (), max(1, total - limit), min(limit, total - 1) + 1)
        return jnp.stack([one, total - one])
    tallies = jnp.asarray(split_up(amount, total, limit, skew), jnp.int32)
    twos = (amount - 1) // 2
    giver, receiver = tallies[1:1 + 2 * twos:2], tallies[2:2 + 2 * twos:2]
    room = jnp.minimum(giver - 1, limit - receiver)
    passed = jax.random.randint(jax.random.fold_in(rng, 1), (twos,), 0, 1 << 20) % (room + 1)
    tallies = tallies.at[1:1 + 2 * twos:2].set(giver - passed).at[2:2 + 2 * twos:2].set(receiver + passed)
    return tallies[jax.random.permutation(jax.random.fold_in(rng, 2), amount)]


def gaussian(rng, extent, spread, most, pieces=(), kind=jnp.bfloat16):
    level = block_scale(rng, extent, pieces, -0.22, 0.18) if pieces else 1.0
    entries = jax.random.normal(rng, extent, jnp.float32) * spread * level
    return jnp.minimum(jnp.maximum(entries, -most), most).astype(kind)


def setup_inputs(seed: int = 0) -> dict:
    keys = jax.random.split(jax.random.key(seed), 12)
    return {
        "tokens": gaussian(keys[0], (TOKENS, D), 1.0, 6.0, ((0, 32), (1, 8))),
        "norm_gain": jnp.clip(1.0 + 0.1 * jax.random.normal(keys[1], (D,), jnp.float32), 0.5, 1.5).astype(jnp.bfloat16),
        "norm_bias": gaussian(keys[2], (D,), 0.3, 4.0),
        "w_query": gaussian(keys[3], (D, HEADS * HD), (D // 8) ** -0.5, 0.25, ((1, 8),)),
        "w_keyval": gaussian(keys[4], (D, 2, HEADS * HD), D ** -0.5, 0.09375, ((2, 8),)),
        "w_out": gaussian(keys[5], (HEADS * HD, D), (HEADS * HD) ** -0.5, 0.125, ((0, 8),)),
        "prefix_key": draw_prefix_key(jax.random.fold_in(keys[11], 71), 0),
        "prefix_value": gaussian(keys[7], (PREFIX, HEADS * HD), 1.0, 6.0, ((0, 32), (1, 8))),
        "lengths": uneven_parts(keys[8], REQS, TOKENS, MOST, 2).astype(jnp.int32),
        "context": plant(jax.random.randint(keys[9], (REQS,), PREFIX // 32, PREFIX + 1), jax.random.fold_in(keys[9], 1), PREFIX // 32, PREFIX).astype(jnp.int32),
        "prefix_place": jax.random.permutation(keys[10], PBLOCKS).astype(jnp.int32),
    }


NEG_FILL = -1e+30

def layer_norm(rows_in, norm_gain, norm_bias):
    as_float = rows_in.astype(jnp.float32)
    row_mean = lax.optimization_barrier(jnp.mean(as_float, -1, keepdims=True))
    centered = as_float - row_mean
    row_var = lax.optimization_barrier(jnp.mean(centered * centered, -1, keepdims=True))
    scaled = centered * lax.rsqrt(row_var + 1e-05)
    return (scaled * norm_gain.astype(jnp.float32) + norm_bias.astype(jnp.float32)).astype(jnp.bfloat16)

def rotate(column_block, position):
    head_dim = column_block.shape[-1]
    half_rot = head_dim // 8
    inverse_freq = jnp.power(jnp.float32(10000.0), -jnp.arange(half_rot, dtype=jnp.float32) * (8.0 / head_dim))
    angles = position.astype(jnp.float32)[:, None] * inverse_freq[None, :]
    cosine = jnp.cos(angles)[:, None, :]
    sines = jnp.sin(angles)[:, None, :]
    first_half = column_block[..., :half_rot]
    second = column_block[..., half_rot:2 * half_rot]
    return jnp.concatenate([first_half * cosine - second * sines, second * cosine + first_half * sines, column_block[..., 2 * half_rot:]], -1)

def request_info(global_index, lengths, context):
    request_end = jnp.cumsum(lengths).astype(jnp.int32)
    starts = (request_end - lengths).astype(jnp.int32)
    inside = ((global_index[:, None] >= starts[None, :]) & (global_index[:, None] < request_end[None, :])).astype(jnp.int32)
    labels = jnp.arange(lengths.shape[0], dtype=jnp.int32) + 1
    request = (lax.optimization_barrier(jnp.sum(inside * labels[None, :], 1)) - 1).astype(jnp.int32)
    cached_len = lax.optimization_barrier(jnp.sum(inside * context[None, :], 1)).astype(jnp.int32)
    position = (lax.optimization_barrier(jnp.sum(inside * (context - starts)[None, :], 1)) + global_index).astype(jnp.int32)
    return (request, cached_len, position)

def reference(tokens, norm_gain, norm_bias, w_query, w_keyval, w_out, prefix_key, prefix_value, lengths, context, prefix_place):
    token_count = tokens.shape[0]
    feature_count = tokens.shape[1]
    head_count = w_query.shape[1] // HD
    normed = layer_norm(tokens, norm_gain, norm_bias)
    global_index = jnp.arange(token_count, dtype=jnp.int32)
    request, cached_len, position = request_info(global_index, lengths, context)
    query_raw = jnp.dot(normed, w_query, preferred_element_type=jnp.float32).reshape(token_count, head_count, HD)
    key_value_raw = jnp.dot(normed, w_keyval.reshape(feature_count, -1), preferred_element_type=jnp.float32).reshape(token_count, 2, head_count, HD)
    queries = rotate(query_raw, position).astype(jnp.bfloat16)
    key_rows = rotate(key_value_raw[:, 0], position).astype(jnp.bfloat16)
    values = key_value_raw[:, 1].astype(jnp.bfloat16)
    prefix_position = (prefix_place[:, None] * PBLOCK + jnp.arange(PBLOCK, dtype=jnp.int32)[None, :]).reshape(-1).astype(jnp.int32)
    prefix_keys = prefix_key.reshape(PREFIX, head_count, HD)
    prefix_values = prefix_value.reshape(PREFIX, head_count, HD)
    padded_keys = jnp.concatenate([jnp.zeros((MOST, head_count, HD), jnp.bfloat16), key_rows], 0)
    padded_values = jnp.concatenate([jnp.zeros((MOST, head_count, HD), jnp.bfloat16), values], 0)
    padded_request = jnp.concatenate([-jnp.ones((MOST,), jnp.int32), request], 0)
    block_rows = math.gcd(token_count, 256)
    scale = 1.0 / math.sqrt(HD)

    def one_block(first_row):
        block_queries = lax.dynamic_slice_in_dim(queries, first_row, block_rows, 0)
        block_request = lax.dynamic_slice_in_dim(request, first_row, block_rows, 0)
        block_cached = lax.dynamic_slice_in_dim(cached_len, first_row, block_rows, 0)
        block_index = first_row + jnp.arange(block_rows, dtype=jnp.int32)
        window_keys = lax.dynamic_slice_in_dim(padded_keys, first_row, MOST + block_rows, 0)
        window_values = lax.dynamic_slice_in_dim(padded_values, first_row, MOST + block_rows, 0)
        window_request = lax.dynamic_slice_in_dim(padded_request, first_row, MOST + block_rows, 0)
        window_index = first_row - MOST + jnp.arange(MOST + block_rows, dtype=jnp.int32)
        sees_prefix = prefix_position[None, :] < block_cached[:, None]
        sees_suffix = (window_request[None, :] == block_request[:, None]) & (window_index[None, :] <= block_index[:, None])
        visible = jnp.concatenate([sees_prefix, sees_suffix], 1)[:, None, :]
        all_keys = jnp.concatenate([prefix_keys, window_keys], 0)
        all_values = jnp.concatenate([prefix_values, window_values], 0)
        scores = jnp.einsum('qhd,khd->qhk', block_queries.astype(jnp.float32), all_keys.astype(jnp.float32)) * scale
        row_max = lax.optimization_barrier(jnp.max(jnp.where(visible, scores, NEG_FILL), -1, keepdims=True))
        exp_terms = jnp.where(visible, jnp.exp(scores - row_max), 0.0)
        row_sum = lax.optimization_barrier(jnp.sum(exp_terms, -1))
        weights = exp_terms.astype(jnp.bfloat16)
        weighted = jnp.einsum('qhk,khd->qhd', weights.astype(jnp.float32), all_values.astype(jnp.float32))
        return (weighted / row_sum[..., None]).astype(jnp.bfloat16).reshape(block_rows, head_count * HD)
    block_starts = jnp.arange(0, token_count, block_rows, dtype=jnp.int32)
    heads_out = lax.map(one_block, block_starts).reshape(token_count, head_count * HD)
    return jnp.dot(heads_out, w_out, preferred_element_type=jnp.float32).astype(jnp.bfloat16)
```

```python
import math

import jax
import jax.numpy as jnp
from jax import lax
from jax.sharding import PartitionSpec as P

HD = 128
PBLOCK = 128


NEG_FILL = -1e30


def layer_norm(rows_in, norm_gain, norm_bias):
    as_float = rows_in.astype(jnp.float32)
    row_mean = jnp.mean(as_float, -1, keepdims=True)
    centered = as_float - row_mean
    row_var = jnp.mean(centered * centered, -1, keepdims=True)
    scaled = centered * lax.rsqrt(row_var + 1e-05)
    return (scaled * norm_gain.astype(jnp.float32) + norm_bias.astype(jnp.float32)).astype(
        jnp.bfloat16
    )


def rotate(column_block, position):
    head_dim = column_block.shape[-1]
    half_rot = head_dim // 8
    inverse_freq = jnp.power(
        jnp.float32(10000.0), -jnp.arange(half_rot, dtype=jnp.float32) * (8.0 / head_dim)
    )
    angles = position.astype(jnp.float32)[:, None] * inverse_freq[None, :]
    cosine = jnp.cos(angles)[:, None, :]
    sines = jnp.sin(angles)[:, None, :]
    first_half = column_block[..., :half_rot]
    second = column_block[..., half_rot : 2 * half_rot]
    return jnp.concatenate(
        [
            first_half * cosine - second * sines,
            second * cosine + first_half * sines,
            column_block[..., 2 * half_rot :],
        ],
        -1,
    )


def request_info(global_index, lengths, context):
    request_end = jnp.cumsum(lengths)
    starts = request_end - lengths
    inside = (
        (global_index[:, None] >= starts[None, :]) & (global_index[:, None] < request_end[None, :])
    ).astype(jnp.int32)
    labels = jnp.arange(lengths.shape[0], dtype=jnp.int32) + 1
    request = jnp.sum(inside * labels[None, :], 1) - 1
    cached_len = jnp.sum(inside * context[None, :], 1)
    position = jnp.sum(inside * (context - starts)[None, :], 1) + global_index
    return (request, cached_len, position)


def masked_softmax_attention(queries, key_sets, value_sets, visible_sets):
    scale = 1.0 / math.sqrt(queries.shape[-1])
    score_sets = [
        jnp.einsum("qhd,khd->hqk", queries, keys, preferred_element_type=jnp.float32) * scale
        for keys in key_sets
    ]
    row_max = None
    for scores, visible in zip(score_sets, visible_sets):
        part = jnp.max(jnp.where(visible[None], scores, NEG_FILL), -1)
        row_max = part if row_max is None else jnp.maximum(row_max, part)
    row_sum = 0.0
    weighted = 0.0
    for scores, visible, values in zip(score_sets, visible_sets, value_sets):
        probs = jnp.where(visible[None], jnp.exp(scores - row_max[..., None]), 0.0)
        row_sum = row_sum + jnp.sum(probs, -1)
        weighted = weighted + jnp.einsum(
            "hqk,khd->hqd", probs.astype(jnp.bfloat16), values, preferred_element_type=jnp.float32
        )
    return weighted / row_sum[..., None]


SUFFIX_SHARDS = 5


def body(
    tokens,
    norm_gain,
    norm_bias,
    w_query,
    w_keyval,
    w_out,
    prefix_key,
    prefix_value,
    lengths,
    context,
    prefix_place,
):
    prefix_rows = prefix_key.shape[0]
    local_heads = w_query.shape[1] // HD
    prefix_both = lax.all_gather(
        jnp.stack([prefix_key, prefix_value], 0), "seq", axis=1, tiled=True
    )
    gathered = lax.all_gather(tokens, "mp", axis=1, tiled=True)
    token_count = gathered.shape[0]
    feature_count = gathered.shape[1]
    normed = layer_norm(gathered, norm_gain, norm_bias)
    seq_index = lax.axis_index("seq")
    seq_count = lax.psum(1, "seq")
    global_index = seq_index * token_count + jnp.arange(token_count, dtype=jnp.int32)
    request, cached_len, position = request_info(global_index, lengths, context)
    query_raw = jnp.dot(normed, w_query, preferred_element_type=jnp.float32).reshape(
        token_count, local_heads, HD
    )
    key_value_raw = jnp.dot(
        normed, w_keyval.reshape(feature_count, -1), preferred_element_type=jnp.float32
    ).reshape(token_count, 2, local_heads, HD)
    queries = rotate(query_raw, position).astype(jnp.bfloat16)
    own_keys = rotate(key_value_raw[:, 0], position).astype(jnp.bfloat16)
    own_values = key_value_raw[:, 1].astype(jnp.bfloat16)
    key_value = jnp.stack([own_keys, own_values], 0)

    window = [key_value]
    for shift in range(1, SUFFIX_SHARDS):
        pairs = [(i, i + shift) for i in range(seq_count - shift)]
        window.insert(0, lax.ppermute(key_value, "seq", pairs))
    window = jnp.concatenate(window, 1)
    window_count = window.shape[1]
    key_index = (seq_index - (SUFFIX_SHARDS - 1)) * token_count + jnp.arange(
        window_count, dtype=jnp.int32
    )
    key_request = request_info(key_index, lengths, context)[0]
    sees_suffix = (
        (key_index[None, :] >= 0)
        & (key_request[None, :] == request[:, None])
        & (key_index[None, :] <= global_index[:, None])
    )

    prefix_all = prefix_both.shape[1]
    prefix_position = (
        prefix_place[:, None] * PBLOCK + jnp.arange(PBLOCK, dtype=jnp.int32)[None, :]
    ).reshape(-1)
    sees_prefix = prefix_position[None, :] < cached_len[:, None]
    prefix_keys = prefix_both[0].reshape(prefix_all, local_heads, HD)
    prefix_values = prefix_both[1].reshape(prefix_all, local_heads, HD)

    attended = masked_softmax_attention(
        queries,
        (prefix_keys, window[0]),
        (prefix_values, window[1]),
        (sees_prefix, sees_suffix),
    )
    heads_out = (
        attended.astype(jnp.bfloat16).transpose(1, 0, 2).reshape(token_count, local_heads * HD)
    )
    summed = lax.psum_scatter(
        jnp.dot(heads_out, w_out, preferred_element_type=jnp.float32).astype(jnp.bfloat16),
        "mp",
        scatter_dimension=0,
        tiled=True,
    )
    return summed


def solution(mesh):
    return jax.shard_map(
        body,
        mesh=mesh,
        in_specs=(
            P("seq", "mp"),
            P(),
            P(),
            P(None, "mp"),
            P(None, None, "mp"),
            P("mp", None),
            P("seq", "mp"),
            P("seq", "mp"),
            P(),
            P(),
            P(),
        ),
        out_specs=P(("seq", "mp"), None),
        check_vma=False,
    )
```

```python
import math

import jax
import jax.numpy as jnp
from jax import lax
from jax.sharding import PartitionSpec as P

HD = 128
PBLOCK = 128


NEG_FILL = -1e30


def layer_norm(rows_in, norm_gain, norm_bias):
    as_float = rows_in.astype(jnp.float32)
    row_mean = jnp.mean(as_float, -1, keepdims=True)
    centered = as_float - row_mean
    row_var = jnp.mean(centered * centered, -1, keepdims=True)
    scaled = centered * lax.rsqrt(row_var + 1e-05)
    return (scaled * norm_gain.astype(jnp.float32) + norm_bias.astype(jnp.float32)).astype(
        jnp.bfloat16
    )


def rotate(column_block, position):
    head_dim = column_block.shape[-1]
    half_rot = head_dim // 8
    inverse_freq = jnp.power(
        jnp.float32(10000.0), -jnp.arange(half_rot, dtype=jnp.float32) * (8.0 / head_dim)
    )
    angles = position.astype(jnp.float32)[:, None] * inverse_freq[None, :]
    cosine = jnp.cos(angles)[:, None, :]
    sines = jnp.sin(angles)[:, None, :]
    first_half = column_block[..., :half_rot]
    second = column_block[..., half_rot : 2 * half_rot]
    return jnp.concatenate(
        [
            first_half * cosine - second * sines,
            second * cosine + first_half * sines,
            column_block[..., 2 * half_rot :],
        ],
        -1,
    )


def request_info(global_index, lengths, context):
    request_end = jnp.cumsum(lengths)
    starts = request_end - lengths
    inside = (
        (global_index[:, None] >= starts[None, :]) & (global_index[:, None] < request_end[None, :])
    ).astype(jnp.int32)
    labels = jnp.arange(lengths.shape[0], dtype=jnp.int32) + 1
    request = jnp.sum(inside * labels[None, :], 1) - 1
    cached_len = jnp.sum(inside * context[None, :], 1)
    position = jnp.sum(inside * (context - starts)[None, :], 1) + global_index
    return (request, cached_len, position)


def masked_softmax_attention(queries, key_sets, value_sets, visible_sets):
    scale = 1.0 / math.sqrt(queries.shape[-1])
    score_sets = [
        jnp.einsum("qhd,khd->hqk", queries, keys, preferred_element_type=jnp.float32) * scale
        for keys in key_sets
    ]
    row_max = None
    for scores, visible in zip(score_sets, visible_sets):
        part = jnp.max(jnp.where(visible[None], scores, NEG_FILL), -1)
        row_max = part if row_max is None else jnp.maximum(row_max, part)
    row_sum = 0.0
    weighted = 0.0
    for scores, visible, values in zip(score_sets, visible_sets, value_sets):
        probs = jnp.where(visible[None], jnp.exp(scores - row_max[..., None]), 0.0)
        row_sum = row_sum + jnp.sum(probs, -1)
        weighted = weighted + jnp.einsum(
            "hqk,khd->hqd", probs.astype(jnp.bfloat16), values, preferred_element_type=jnp.float32
        )
    return weighted / row_sum[..., None]


SUFFIX_SHARDS = 5


def gather_features(tokens):
    mp_count = lax.psum(1, "mp")
    ring = mp_count // 2
    mp_index = lax.axis_index("mp")
    partner = lax.ppermute(tokens, "mp", [(i, i ^ 1) for i in range(mp_count)])
    pair = jnp.where(
        mp_index % 2 == 0,
        jnp.concatenate([tokens, partner], 1),
        jnp.concatenate([partner, tokens], 1),
    )
    blocks = [pair]
    for shift in range(1, ring):
        blocks.append(
            lax.ppermute(pair, "mp", [(i, (i + 2 * shift) % mp_count) for i in range(mp_count)])
        )
    ring_index = mp_index // 2
    order = (ring_index - jnp.arange(ring, dtype=jnp.int32)) % ring
    stacked = jnp.stack(blocks, 0)[order]
    return stacked.transpose(1, 0, 2).reshape(tokens.shape[0], -1)


def body(
    tokens,
    norm_gain,
    norm_bias,
    w_query,
    w_keyval,
    w_out,
    prefix_key,
    prefix_value,
    lengths,
    context,
    prefix_place,
):
    prefix_rows = prefix_key.shape[0]
    local_heads = w_query.shape[1] // HD
    prefix_both = lax.all_gather(
        jnp.stack([prefix_key, prefix_value], 0), "seq", axis=1, tiled=True
    )
    gathered = gather_features(tokens)
    token_count = gathered.shape[0]
    feature_count = gathered.shape[1]
    normed = layer_norm(gathered, norm_gain, norm_bias)
    seq_index = lax.axis_index("seq")
    seq_count = lax.psum(1, "seq")
    global_index = seq_index * token_count + jnp.arange(token_count, dtype=jnp.int32)
    request, cached_len, position = request_info(global_index, lengths, context)
    query_raw = jnp.dot(normed, w_query, preferred_element_type=jnp.float32).reshape(
        token_count, local_heads, HD
    )
    key_value_raw = jnp.dot(
        normed, w_keyval.reshape(feature_count, -1), preferred_element_type=jnp.float32
    ).reshape(token_count, 2, local_heads, HD)
    queries = rotate(query_raw, position).astype(jnp.bfloat16)
    own_keys = rotate(key_value_raw[:, 0], position).astype(jnp.bfloat16)
    own_values = key_value_raw[:, 1].astype(jnp.bfloat16)
    key_value = jnp.stack([own_keys, own_values], 0)

    window = [key_value]
    for shift in range(1, SUFFIX_SHARDS):
        pairs = [(i, i + shift) for i in range(seq_count - shift)]
        window.insert(0, lax.ppermute(key_value, "seq", pairs))
    window = jnp.concatenate(window, 1)
    window_count = window.shape[1]
    key_index = (seq_index - (SUFFIX_SHARDS - 1)) * token_count + jnp.arange(
        window_count, dtype=jnp.int32
    )
    key_request = request_info(key_index, lengths, context)[0]
    sees_suffix = (
        (key_index[None, :] >= 0)
        & (key_request[None, :] == request[:, None])
        & (key_index[None, :] <= global_index[:, None])
    )

    prefix_all = prefix_both.shape[1]
    prefix_position = (
        prefix_place[:, None] * PBLOCK + jnp.arange(PBLOCK, dtype=jnp.int32)[None, :]
    ).reshape(-1)
    sees_prefix = prefix_position[None, :] < cached_len[:, None]
    prefix_keys = prefix_both[0].reshape(prefix_all, local_heads, HD)
    prefix_values = prefix_both[1].reshape(prefix_all, local_heads, HD)

    attended = masked_softmax_attention(
        queries,
        (prefix_keys, window[0]),
        (prefix_values, window[1]),
        (sees_prefix, sees_suffix),
    )
    heads_out = (
        attended.astype(jnp.bfloat16).transpose(1, 0, 2).reshape(token_count, local_heads * HD)
    )
    partial = jnp.dot(heads_out, w_out, preferred_element_type=jnp.float32).astype(jnp.bfloat16)
    mp_count = lax.psum(1, "mp")
    exchanged = lax.all_to_all(
        partial.reshape(mp_count, token_count // mp_count, -1), "mp", 0, 0, tiled=False
    )
    return jnp.sum(exchanged.astype(jnp.float32), 0).astype(jnp.bfloat16)


def solution(mesh):
    return jax.shard_map(
        body,
        mesh=mesh,
        in_specs=(
            P("seq", "mp"),
            P(),
            P(),
            P(None, "mp"),
            P(None, None, "mp"),
            P("mp", None),
            P("seq", "mp"),
            P("seq", "mp"),
            P(),
            P(),
            P(),
        ),
        out_specs=P(("seq", "mp"), None),
        check_vma=False,
    )
```

```python
import math

import jax
import jax.numpy as jnp
from jax import lax
from jax.sharding import Mesh, PartitionSpec as P

HD = 128
PBLOCK = 128


NEG_FILL = -1e30


def layer_norm(rows_in, norm_gain, norm_bias):
    as_float = rows_in.astype(jnp.float32)
    row_mean = jnp.mean(as_float, -1, keepdims=True)
    centered = as_float - row_mean
    row_var = jnp.mean(centered * centered, -1, keepdims=True)
    scaled = centered * lax.rsqrt(row_var + 1e-05)
    return (scaled * norm_gain.astype(jnp.float32) + norm_bias.astype(jnp.float32)).astype(
        jnp.bfloat16
    )


def rotate(column_block, position):
    head_dim = column_block.shape[-1]
    half_rot = head_dim // 8
    inverse_freq = jnp.power(
        jnp.float32(10000.0), -jnp.arange(half_rot, dtype=jnp.float32) * (8.0 / head_dim)
    )
    angles = position.astype(jnp.float32)[:, None] * inverse_freq[None, :]
    cosine = jnp.cos(angles)[:, None, :]
    sines = jnp.sin(angles)[:, None, :]
    first_half = column_block[..., :half_rot]
    second = column_block[..., half_rot : 2 * half_rot]
    return jnp.concatenate(
        [
            first_half * cosine - second * sines,
            second * cosine + first_half * sines,
            column_block[..., 2 * half_rot :],
        ],
        -1,
    )


def request_info(global_index, lengths, context):
    request_end = jnp.cumsum(lengths)
    starts = request_end - lengths
    inside = (
        (global_index[:, None] >= starts[None, :]) & (global_index[:, None] < request_end[None, :])
    ).astype(jnp.int32)
    labels = jnp.arange(lengths.shape[0], dtype=jnp.int32) + 1
    request = jnp.sum(inside * labels[None, :], 1) - 1
    cached_len = jnp.sum(inside * context[None, :], 1)
    position = jnp.sum(inside * (context - starts)[None, :], 1) + global_index
    return (request, cached_len, position)


def masked_softmax_attention(queries, key_sets, value_sets, visible_sets):
    scale = 1.0 / math.sqrt(queries.shape[-1])
    score_sets = [
        jnp.einsum("qhd,khd->hqk", queries, keys, preferred_element_type=jnp.float32) * scale
        for keys in key_sets
    ]
    row_max = None
    for scores, visible in zip(score_sets, visible_sets):
        part = jnp.max(jnp.where(visible[None], scores, NEG_FILL), -1)
        row_max = part if row_max is None else jnp.maximum(row_max, part)
    row_sum = 0.0
    weighted = 0.0
    for scores, visible, values in zip(score_sets, visible_sets, value_sets):
        probs = jnp.where(visible[None], jnp.exp(scores - row_max[..., None]), 0.0)
        row_sum = row_sum + jnp.sum(probs, -1)
        weighted = weighted + jnp.einsum(
            "hqk,khd->hqd", probs.astype(jnp.bfloat16), values, preferred_element_type=jnp.float32
        )
    return weighted / row_sum[..., None]


SUFFIX_SHARDS = 5


def gather_features(tokens):
    ring = lax.psum(1, "ring")
    partner = lax.ppermute(tokens, "zh", [(0, 1), (1, 0)])
    pair = jnp.where(
        lax.axis_index("zh") == 0,
        jnp.concatenate([tokens, partner], 1),
        jnp.concatenate([partner, tokens], 1),
    )
    blocks = [pair]
    for shift in range(1, ring):
        blocks.append(lax.ppermute(pair, "ring", [(i, (i + shift) % ring) for i in range(ring)]))
    order = (lax.axis_index("ring") - jnp.arange(ring, dtype=jnp.int32)) % ring
    stacked = jnp.stack(blocks, 0)[order]
    return stacked.transpose(1, 0, 2).reshape(tokens.shape[0], -1)


def body(
    tokens,
    norm_gain,
    norm_bias,
    w_query,
    w_keyval,
    w_out,
    prefix_key,
    prefix_value,
    lengths,
    context,
    prefix_place,
):
    prefix_rows = prefix_key.shape[0]
    local_heads = w_query.shape[1] // HD
    core_index = lax.axis_index("core")
    first_core = core_index == 0
    kept = jnp.where(first_core, prefix_key, prefix_value)
    given = jnp.where(first_core, prefix_value, prefix_key)
    received = lax.ppermute(given, "core", [(0, 1), (1, 0)])
    chip_rows = jnp.where(
        first_core,
        jnp.concatenate([kept, received], 0),
        jnp.concatenate([received, kept], 0),
    )
    gathered_half = lax.all_gather(chip_rows, "chip", axis=0, tiled=True)
    other_half = lax.ppermute(gathered_half, "core", [(0, 1), (1, 0)])
    prefix_k_all = jnp.where(first_core, gathered_half, other_half)
    prefix_v_all = jnp.where(first_core, other_half, gathered_half)
    gathered = gather_features(tokens)
    token_count = gathered.shape[0]
    feature_count = gathered.shape[1]
    normed = layer_norm(gathered, norm_gain, norm_bias)
    seq_index = lax.axis_index(SEQ)
    seq_count = lax.psum(1, SEQ)
    global_index = seq_index * token_count + jnp.arange(token_count, dtype=jnp.int32)
    request, cached_len, position = request_info(global_index, lengths, context)
    query_raw = jnp.dot(normed, w_query, preferred_element_type=jnp.float32).reshape(
        token_count, local_heads, HD
    )
    key_value_raw = jnp.dot(
        normed, w_keyval.reshape(feature_count, -1), preferred_element_type=jnp.float32
    ).reshape(token_count, 2, local_heads, HD)
    queries = rotate(query_raw, position).astype(jnp.bfloat16)
    own_keys = rotate(key_value_raw[:, 0], position).astype(jnp.bfloat16)
    own_values = key_value_raw[:, 1].astype(jnp.bfloat16)
    key_value = jnp.stack([own_keys, own_values], 0)

    window = [key_value]
    for shift in range(1, SUFFIX_SHARDS):
        pairs = [(i, i + shift) for i in range(seq_count - shift)]
        window.insert(0, lax.ppermute(key_value, SEQ, pairs))
    window = jnp.concatenate(window, 1)
    window_count = window.shape[1]
    key_index = (seq_index - (SUFFIX_SHARDS - 1)) * token_count + jnp.arange(
        window_count, dtype=jnp.int32
    )
    key_request = request_info(key_index, lengths, context)[0]
    sees_suffix = (
        (key_index[None, :] >= 0)
        & (key_request[None, :] == request[:, None])
        & (key_index[None, :] <= global_index[:, None])
    )

    prefix_all = prefix_k_all.shape[0]
    prefix_position = (
        prefix_place[:, None] * PBLOCK + jnp.arange(PBLOCK, dtype=jnp.int32)[None, :]
    ).reshape(-1)
    sees_prefix = prefix_position[None, :] < cached_len[:, None]
    prefix_keys = prefix_k_all.reshape(prefix_all, local_heads, HD)
    prefix_values = prefix_v_all.reshape(prefix_all, local_heads, HD)

    attended = masked_softmax_attention(
        queries,
        (prefix_keys, window[0]),
        (prefix_values, window[1]),
        (sees_prefix, sees_suffix),
    )
    heads_out = (
        attended.astype(jnp.bfloat16).transpose(1, 0, 2).reshape(token_count, local_heads * HD)
    )
    partial = jnp.dot(heads_out, w_out, preferred_element_type=jnp.float32).astype(jnp.bfloat16)
    ring = lax.psum(1, "ring")
    pairs = lax.psum(1, "zh")
    by_ring = lax.all_to_all(
        partial.reshape(ring, token_count // ring, -1), "ring", 0, 0, tiled=False
    )
    ring_sum = jnp.sum(by_ring.astype(jnp.float32), 0)
    by_pair = lax.all_to_all(
        ring_sum.reshape(pairs, token_count // (ring * pairs), -1), "zh", 0, 0, tiled=False
    )
    return jnp.sum(by_pair, 0).astype(jnp.bfloat16)


SEQ = ("chip", "core")
MP = ("ring", "zh")


def solution(mesh):
    seq_count, mp_count = mesh.devices.shape
    split_mesh = Mesh(
        mesh.devices.reshape(seq_count // 2, 2, mp_count // 2, 2), ("chip", "core", "ring", "zh")
    )
    return jax.shard_map(
        body,
        mesh=split_mesh,
        in_specs=(
            P(SEQ, MP),
            P(),
            P(),
            P(None, MP),
            P(None, None, MP),
            P(MP, None),
            P(SEQ, MP),
            P(SEQ, MP),
            P(),
            P(),
            P(),
        ),
        out_specs=P(SEQ + MP, None),
        check_vma=False,
    )
```

```python
import math

import jax
import jax.numpy as jnp
from jax import lax
from jax.sharding import PartitionSpec as P

HD = 128
PBLOCK = 128


NEG_FILL = -1e30


def layer_norm(rows_in, norm_gain, norm_bias):
    as_float = rows_in.astype(jnp.float32)
    row_mean = jnp.mean(as_float, -1, keepdims=True)
    centered = as_float - row_mean
    row_var = jnp.mean(centered * centered, -1, keepdims=True)
    scaled = centered * lax.rsqrt(row_var + 1e-05)
    return (scaled * norm_gain.astype(jnp.float32) + norm_bias.astype(jnp.float32)).astype(
        jnp.bfloat16
    )


def rotate(column_block, position):
    head_dim = column_block.shape[-1]
    half_rot = head_dim // 8
    inverse_freq = jnp.power(
        jnp.float32(10000.0), -jnp.arange(half_rot, dtype=jnp.float32) * (8.0 / head_dim)
    )
    angles = position.astype(jnp.float32)[:, None] * inverse_freq[None, :]
    cosine = jnp.cos(angles)[:, None, :]
    sines = jnp.sin(angles)[:, None, :]
    first_half = column_block[..., :half_rot]
    second = column_block[..., half_rot : 2 * half_rot]
    return jnp.concatenate(
        [
            first_half * cosine - second * sines,
            second * cosine + first_half * sines,
            column_block[..., 2 * half_rot :],
        ],
        -1,
    )


def request_info(global_index, lengths, context):
    request_end = jnp.cumsum(lengths)
    starts = request_end - lengths
    inside = (
        (global_index[:, None] >= starts[None, :]) & (global_index[:, None] < request_end[None, :])
    ).astype(jnp.int32)
    labels = jnp.arange(lengths.shape[0], dtype=jnp.int32) + 1
    request = jnp.sum(inside * labels[None, :], 1) - 1
    cached_len = jnp.sum(inside * context[None, :], 1)
    position = jnp.sum(inside * (context - starts)[None, :], 1) + global_index
    return (request, cached_len, position)


def masked_softmax_attention(queries, key_sets, value_sets, visible_sets):
    scale = 1.0 / math.sqrt(queries.shape[-1])
    score_sets = [
        jnp.einsum("qhd,khd->hqk", queries, keys, preferred_element_type=jnp.float32) * scale
        for keys in key_sets
    ]
    row_max = None
    for scores, visible in zip(score_sets, visible_sets):
        part = jnp.max(jnp.where(visible[None], scores, NEG_FILL), -1)
        row_max = part if row_max is None else jnp.maximum(row_max, part)
    row_sum = 0.0
    weighted = 0.0
    for scores, visible, values in zip(score_sets, visible_sets, value_sets):
        probs = jnp.where(visible[None], jnp.exp(scores - row_max[..., None]), 0.0)
        row_sum = row_sum + jnp.sum(probs, -1)
        weighted = weighted + jnp.einsum(
            "hqk,khd->hqd", probs.astype(jnp.bfloat16), values, preferred_element_type=jnp.float32
        )
    return weighted / row_sum[..., None]


SUFFIX_SHARDS = 5


def gather_features(tokens):
    mp_count = lax.psum(1, "mp")
    ring = mp_count // 2
    mp_index = lax.axis_index("mp")
    partner = lax.ppermute(tokens, "mp", [(i, i ^ 1) for i in range(mp_count)])
    pair = jnp.where(
        mp_index % 2 == 0,
        jnp.concatenate([tokens, partner], 1),
        jnp.concatenate([partner, tokens], 1),
    )
    blocks = [pair]
    for shift in range(1, ring):
        blocks.append(
            lax.ppermute(pair, "mp", [(i, (i + 2 * shift) % mp_count) for i in range(mp_count)])
        )
    ring_index = mp_index // 2
    order = (ring_index - jnp.arange(ring, dtype=jnp.int32)) % ring
    stacked = jnp.stack(blocks, 0)[order]
    return stacked.transpose(1, 0, 2).reshape(tokens.shape[0], -1)


def body(
    tokens,
    norm_gain,
    norm_bias,
    w_query,
    w_keyval,
    w_out,
    prefix_key,
    prefix_value,
    lengths,
    context,
    prefix_place,
):
    prefix_rows = prefix_key.shape[0]
    local_heads = w_query.shape[1] // HD
    prefix_k_all, prefix_v_all = lax.all_gather(
        (prefix_key, prefix_value), "seq", axis=0, tiled=True
    )
    gathered = gather_features(tokens)
    token_count = gathered.shape[0]
    feature_count = gathered.shape[1]
    normed = layer_norm(gathered, norm_gain, norm_bias)
    seq_index = lax.axis_index("seq")
    seq_count = lax.psum(1, "seq")
    global_index = seq_index * token_count + jnp.arange(token_count, dtype=jnp.int32)
    request, cached_len, position = request_info(global_index, lengths, context)
    query_raw = jnp.dot(normed, w_query, preferred_element_type=jnp.float32).reshape(
        token_count, local_heads, HD
    )
    key_value_raw = jnp.dot(
        normed, w_keyval.reshape(feature_count, -1), preferred_element_type=jnp.float32
    ).reshape(token_count, 2, local_heads, HD)
    queries = rotate(query_raw, position).astype(jnp.bfloat16)
    own_keys = rotate(key_value_raw[:, 0], position).astype(jnp.bfloat16)
    own_values = key_value_raw[:, 1].astype(jnp.bfloat16)
    key_value = jnp.stack([own_keys, own_values], 0)

    window = [key_value]
    for shift in range(1, SUFFIX_SHARDS):
        pairs = [(i, i + shift) for i in range(seq_count - shift)]
        window.insert(0, lax.ppermute(key_value, "seq", pairs))
    window = jnp.concatenate(window, 1)
    window_count = window.shape[1]
    key_index = (seq_index - (SUFFIX_SHARDS - 1)) * token_count + jnp.arange(
        window_count, dtype=jnp.int32
    )
    key_request = request_info(key_index, lengths, context)[0]
    sees_suffix = (
        (key_index[None, :] >= 0)
        & (key_request[None, :] == request[:, None])
        & (key_index[None, :] <= global_index[:, None])
    )

    prefix_all = prefix_k_all.shape[0]
    prefix_position = (
        prefix_place[:, None] * PBLOCK + jnp.arange(PBLOCK, dtype=jnp.int32)[None, :]
    ).reshape(-1)
    sees_prefix = prefix_position[None, :] < cached_len[:, None]
    prefix_keys = prefix_k_all.reshape(prefix_all, local_heads, HD)
    prefix_values = prefix_v_all.reshape(prefix_all, local_heads, HD)

    attended = masked_softmax_attention(
        queries,
        (prefix_keys, window[0]),
        (prefix_values, window[1]),
        (sees_prefix, sees_suffix),
    )
    heads_out = (
        attended.astype(jnp.bfloat16).transpose(1, 0, 2).reshape(token_count, local_heads * HD)
    )
    partial = jnp.dot(heads_out, w_out, preferred_element_type=jnp.float32).astype(jnp.bfloat16)
    mp_count = lax.psum(1, "mp")
    exchanged = lax.all_to_all(
        partial.reshape(mp_count, token_count // mp_count, -1), "mp", 0, 0, tiled=False
    )
    return jnp.sum(exchanged.astype(jnp.float32), 0).astype(jnp.bfloat16)


def solution(mesh):
    return jax.shard_map(
        body,
        mesh=mesh,
        in_specs=(
            P("seq", "mp"),
            P(),
            P(),
            P(None, "mp"),
            P(None, None, "mp"),
            P("mp", None),
            P("seq", "mp"),
            P("seq", "mp"),
            P(),
            P(),
            P(),
        ),
        out_specs=P(("seq", "mp"), None),
        check_vma=False,
    )
```

```python
import math

import jax
import jax.numpy as jnp
from jax import lax
from jax.sharding import PartitionSpec as P

HD = 128
PBLOCK = 128


NEG_FILL = -1e30


def layer_norm(rows_in, norm_gain, norm_bias):
    as_float = rows_in.astype(jnp.float32)
    row_mean = jnp.mean(as_float, -1, keepdims=True)
    centered = as_float - row_mean
    row_var = jnp.mean(centered * centered, -1, keepdims=True)
    scaled = centered * lax.rsqrt(row_var + 1e-05)
    return (scaled * norm_gain.astype(jnp.float32) + norm_bias.astype(jnp.float32)).astype(
        jnp.bfloat16
    )


def rotate(column_block, position):
    head_dim = column_block.shape[-1]
    half_rot = head_dim // 8
    inverse_freq = jnp.power(
        jnp.float32(10000.0), -jnp.arange(half_rot, dtype=jnp.float32) * (8.0 / head_dim)
    )
    angles = position.astype(jnp.float32)[:, None] * inverse_freq[None, :]
    cosine = jnp.cos(angles)[:, None, :]
    sines = jnp.sin(angles)[:, None, :]
    first_half = column_block[..., :half_rot]
    second = column_block[..., half_rot : 2 * half_rot]
    return jnp.concatenate(
        [
            first_half * cosine - second * sines,
            second * cosine + first_half * sines,
            column_block[..., 2 * half_rot :],
        ],
        -1,
    )


def request_info(global_index, lengths, context):
    request_end = jnp.cumsum(lengths)
    starts = request_end - lengths
    inside = (
        (global_index[:, None] >= starts[None, :]) & (global_index[:, None] < request_end[None, :])
    ).astype(jnp.int32)
    labels = jnp.arange(lengths.shape[0], dtype=jnp.int32) + 1
    request = jnp.sum(inside * labels[None, :], 1) - 1
    cached_len = jnp.sum(inside * context[None, :], 1)
    position = jnp.sum(inside * (context - starts)[None, :], 1) + global_index
    return (request, cached_len, position)


def masked_softmax_attention(queries, key_sets, value_sets, visible_sets):
    scale = 1.0 / math.sqrt(queries.shape[-1])
    score_sets = [
        jnp.einsum("qhd,khd->hqk", queries, keys, preferred_element_type=jnp.float32) * scale
        for keys in key_sets
    ]
    row_max = None
    for scores, visible in zip(score_sets, visible_sets):
        part = jnp.max(jnp.where(visible[None], scores, NEG_FILL), -1)
        row_max = part if row_max is None else jnp.maximum(row_max, part)
    row_sum = 0.0
    weighted = 0.0
    for scores, visible, values in zip(score_sets, visible_sets, value_sets):
        probs = jnp.where(visible[None], jnp.exp(scores - row_max[..., None]), 0.0)
        row_sum = row_sum + jnp.sum(probs, -1)
        weighted = weighted + jnp.einsum(
            "hqk,khd->hqd", probs.astype(jnp.bfloat16), values, preferred_element_type=jnp.float32
        )
    return weighted / row_sum[..., None]


SUFFIX_SHARDS = 5


def gather_features(tokens):
    mp_count = lax.psum(1, "mp")
    ring = mp_count // 2
    mp_index = lax.axis_index("mp")
    partner = lax.ppermute(tokens, "mp", [(i, i ^ 1) for i in range(mp_count)])
    pair = jnp.where(
        mp_index % 2 == 0,
        jnp.concatenate([tokens, partner], 1),
        jnp.concatenate([partner, tokens], 1),
    )
    blocks = [pair]
    for shift in range(1, ring):
        blocks.append(
            lax.ppermute(pair, "mp", [(i, (i + 2 * shift) % mp_count) for i in range(mp_count)])
        )
    ring_index = mp_index // 2
    order = (ring_index - jnp.arange(ring, dtype=jnp.int32)) % ring
    stacked = jnp.stack(blocks, 0)[order]
    return stacked.transpose(1, 0, 2).reshape(tokens.shape[0], -1)


def body(
    tokens,
    norm_gain,
    norm_bias,
    w_query,
    w_keyval,
    w_out,
    prefix_key,
    prefix_value,
    lengths,
    context,
    prefix_place,
):
    prefix_rows = prefix_key.shape[0]
    local_heads = w_query.shape[1] // HD
    prefix_both = lax.all_gather(
        jnp.stack([prefix_key, prefix_value], 0), "seq", axis=1, tiled=True
    )
    gathered = gather_features(tokens)
    token_count = gathered.shape[0]
    feature_count = gathered.shape[1]
    normed = layer_norm(gathered, norm_gain, norm_bias)
    seq_index = lax.axis_index("seq")
    seq_count = lax.psum(1, "seq")
    global_index = seq_index * token_count + jnp.arange(token_count, dtype=jnp.int32)
    request, cached_len, position = request_info(global_index, lengths, context)
    query_raw = jnp.dot(normed, w_query, preferred_element_type=jnp.float32).reshape(
        token_count, local_heads, HD
    )
    key_value_raw = jnp.dot(
        normed, w_keyval.reshape(feature_count, -1), preferred_element_type=jnp.float32
    ).reshape(token_count, 2, local_heads, HD)
    queries = rotate(query_raw, position).astype(jnp.bfloat16)
    own_keys = rotate(key_value_raw[:, 0], position).astype(jnp.bfloat16)
    own_values = key_value_raw[:, 1].astype(jnp.bfloat16)
    key_value = jnp.stack([own_keys, own_values], 0)

    window = [key_value]
    for shift in range(1, SUFFIX_SHARDS):
        pairs = [(i, i + shift) for i in range(seq_count - shift)]
        window.insert(0, lax.ppermute(key_value, "seq", pairs))
    window = jnp.concatenate(window, 1)
    window_count = window.shape[1]
    key_index = (seq_index - (SUFFIX_SHARDS - 1)) * token_count + jnp.arange(
        window_count, dtype=jnp.int32
    )
    key_request = request_info(key_index, lengths, context)[0]
    sees_suffix = (
        (key_index[None, :] >= 0)
        & (key_request[None, :] == request[:, None])
        & (key_index[None, :] <= global_index[:, None])
    )

    prefix_all = prefix_both.shape[1]
    prefix_position = (
        prefix_place[:, None] * PBLOCK + jnp.arange(PBLOCK, dtype=jnp.int32)[None, :]
    ).reshape(-1)
    sees_prefix = prefix_position[None, :] < cached_len[:, None]
    prefix_keys = prefix_both[0].reshape(prefix_all, local_heads, HD)
    prefix_values = prefix_both[1].reshape(prefix_all, local_heads, HD)

    attended = masked_softmax_attention(
        queries,
        (prefix_keys, window[0]),
        (prefix_values, window[1]),
        (sees_prefix, sees_suffix),
    )
    heads_out = (
        attended.astype(jnp.bfloat16).transpose(1, 0, 2).reshape(token_count, local_heads * HD)
    )
    partial = jnp.dot(heads_out, w_out, preferred_element_type=jnp.float32).astype(jnp.bfloat16)
    mp_count = lax.psum(1, "mp")
    mp_index = lax.axis_index("mp")
    chunks = partial.reshape(mp_count, token_count // mp_count, -1)
    total = chunks[mp_index].astype(jnp.float32)
    for shift in range(1, mp_count):
        outgoing = chunks[(mp_index + shift) % mp_count]
        incoming = lax.ppermute(
            outgoing, "mp", [(i, (i + shift) % mp_count) for i in range(mp_count)]
        )
        total = total + incoming.astype(jnp.float32)
    return total.astype(jnp.bfloat16)


def solution(mesh):
    return jax.shard_map(
        body,
        mesh=mesh,
        in_specs=(
            P("seq", "mp"),
            P(),
            P(),
            P(None, "mp"),
            P(None, None, "mp"),
            P("mp", None),
            P("seq", "mp"),
            P("seq", "mp"),
            P(),
            P(),
            P(),
        ),
        out_specs=P(("seq", "mp"), None),
        check_vma=False,
    )
```

```python
import math

import jax
import jax.numpy as jnp
from jax import lax
from jax.sharding import PartitionSpec as P

HD = 128
PBLOCK = 128


NEG_FILL = -1e30


def layer_norm(rows_in, norm_gain, norm_bias):
    as_float = rows_in.astype(jnp.float32)
    row_mean = jnp.mean(as_float, -1, keepdims=True)
    centered = as_float - row_mean
    row_var = jnp.mean(centered * centered, -1, keepdims=True)
    scaled = centered * lax.rsqrt(row_var + 1e-05)
    return (scaled * norm_gain.astype(jnp.float32) + norm_bias.astype(jnp.float32)).astype(
        jnp.bfloat16
    )


def rotate(column_block, position):
    head_dim = column_block.shape[-1]
    half_rot = head_dim // 8
    inverse_freq = jnp.power(
        jnp.float32(10000.0), -jnp.arange(half_rot, dtype=jnp.float32) * (8.0 / head_dim)
    )
    angles = position.astype(jnp.float32)[:, None] * inverse_freq[None, :]
    cosine = jnp.cos(angles)[:, None, :]
    sines = jnp.sin(angles)[:, None, :]
    first_half = column_block[..., :half_rot]
    second = column_block[..., half_rot : 2 * half_rot]
    return jnp.concatenate(
        [
            first_half * cosine - second * sines,
            second * cosine + first_half * sines,
            column_block[..., 2 * half_rot :],
        ],
        -1,
    )


def request_info(global_index, lengths, context):
    request_end = jnp.cumsum(lengths)
    starts = request_end - lengths
    inside = (
        (global_index[:, None] >= starts[None, :]) & (global_index[:, None] < request_end[None, :])
    ).astype(jnp.int32)
    labels = jnp.arange(lengths.shape[0], dtype=jnp.int32) + 1
    request = jnp.sum(inside * labels[None, :], 1) - 1
    cached_len = jnp.sum(inside * context[None, :], 1)
    position = jnp.sum(inside * (context - starts)[None, :], 1) + global_index
    return (request, cached_len, position)


def masked_softmax_attention(queries, key_sets, value_sets, visible_sets):
    scale = 1.0 / math.sqrt(queries.shape[-1])
    score_sets = [
        jnp.einsum("qhd,khd->hqk", queries, keys, preferred_element_type=jnp.float32) * scale
        for keys in key_sets
    ]
    row_max = None
    for scores, visible in zip(score_sets, visible_sets):
        part = jnp.max(jnp.where(visible[None], scores, NEG_FILL), -1)
        row_max = part if row_max is None else jnp.maximum(row_max, part)
    row_sum = 0.0
    weighted = 0.0
    for scores, visible, values in zip(score_sets, visible_sets, value_sets):
        probs = jnp.where(visible[None], jnp.exp(scores - row_max[..., None]), 0.0)
        row_sum = row_sum + jnp.sum(probs, -1)
        weighted = weighted + jnp.einsum(
            "hqk,khd->hqd", probs.astype(jnp.bfloat16), values, preferred_element_type=jnp.float32
        )
    return weighted / row_sum[..., None]


SUFFIX_SHARDS = 5


def gather_features(tokens):
    mp_count = lax.psum(1, "mp")
    ring = mp_count // 2
    mp_index = lax.axis_index("mp")
    partner = lax.ppermute(tokens, "mp", [(i, i ^ 1) for i in range(mp_count)])
    pair = jnp.where(
        mp_index % 2 == 0,
        jnp.concatenate([tokens, partner], 1),
        jnp.concatenate([partner, tokens], 1),
    )
    blocks = [pair]
    for shift in range(1, ring):
        blocks.append(
            lax.ppermute(pair, "mp", [(i, (i + 2 * shift) % mp_count) for i in range(mp_count)])
        )
    ring_index = mp_index // 2
    order = (ring_index - jnp.arange(ring, dtype=jnp.int32)) % ring
    stacked = jnp.stack(blocks, 0)[order]
    return stacked.transpose(1, 0, 2).reshape(tokens.shape[0], -1)


def body(
    tokens,
    norm_gain,
    norm_bias,
    w_query,
    w_keyval,
    w_out,
    prefix_key,
    prefix_value,
    lengths,
    context,
    prefix_place,
):
    prefix_rows = prefix_key.shape[0]
    local_heads = w_query.shape[1] // HD
    prefix_both = lax.all_gather(
        jnp.stack([prefix_key, prefix_value], 0), "seq", axis=1, tiled=True
    )
    gathered = gather_features(tokens)
    token_count = gathered.shape[0]
    feature_count = gathered.shape[1]
    normed = layer_norm(gathered, norm_gain, norm_bias)
    seq_index = lax.axis_index("seq")
    seq_count = lax.psum(1, "seq")
    global_index = seq_index * token_count + jnp.arange(token_count, dtype=jnp.int32)
    request, cached_len, position = request_info(global_index, lengths, context)
    query_raw = jnp.dot(normed, w_query, preferred_element_type=jnp.float32).reshape(
        token_count, local_heads, HD
    )
    key_value_raw = jnp.dot(
        normed, w_keyval.reshape(feature_count, -1), preferred_element_type=jnp.float32
    ).reshape(token_count, 2, local_heads, HD)
    queries = rotate(query_raw, position).astype(jnp.bfloat16)
    own_keys = rotate(key_value_raw[:, 0], position).astype(jnp.bfloat16)
    own_values = key_value_raw[:, 1].astype(jnp.bfloat16)
    key_value = jnp.stack([own_keys, own_values], 0)

    window = [key_value]
    for shift in range(1, SUFFIX_SHARDS):
        pairs = [(i, i + shift) for i in range(seq_count - shift)]
        window.insert(0, lax.ppermute(key_value, "seq", pairs))
    window = jnp.concatenate(window, 1)
    window_count = window.shape[1]
    key_index = (seq_index - (SUFFIX_SHARDS - 1)) * token_count + jnp.arange(
        window_count, dtype=jnp.int32
    )
    key_request = request_info(key_index, lengths, context)[0]
    sees_suffix = (
        (key_index[None, :] >= 0)
        & (key_request[None, :] == request[:, None])
        & (key_index[None, :] <= global_index[:, None])
    )

    prefix_all = prefix_both.shape[1]
    prefix_position = (
        prefix_place[:, None] * PBLOCK + jnp.arange(PBLOCK, dtype=jnp.int32)[None, :]
    ).reshape(-1)
    sees_prefix = prefix_position[None, :] < cached_len[:, None]
    prefix_keys = prefix_both[0].reshape(prefix_all, local_heads, HD)
    prefix_values = prefix_both[1].reshape(prefix_all, local_heads, HD)

    attended = masked_softmax_attention(
        queries,
        (prefix_keys, window[0]),
        (prefix_values, window[1]),
        (sees_prefix, sees_suffix),
    )
    heads_out = (
        attended.astype(jnp.bfloat16).transpose(1, 0, 2).reshape(token_count, local_heads * HD)
    )
    partial = jnp.dot(heads_out, w_out, preferred_element_type=jnp.float32).astype(jnp.bfloat16)
    mp_count = lax.psum(1, "mp")
    mp_index = lax.axis_index("mp")
    ring = mp_count // 2
    ring_index = mp_index // 2
    chunks = partial.reshape(ring, token_count // ring, -1)
    ring_total = chunks[ring_index].astype(jnp.float32)
    for shift in range(1, ring):
        outgoing = chunks[(ring_index + shift) % ring]
        incoming = lax.ppermute(
            outgoing, "mp", [(i, (i + 2 * shift) % mp_count) for i in range(mp_count)]
        )
        ring_total = ring_total + incoming.astype(jnp.float32)
    halves = ring_total.reshape(2, token_count // mp_count, -1)
    side = mp_index % 2
    swapped = lax.ppermute(halves[1 - side], "mp", [(i, i ^ 1) for i in range(mp_count)])
    total = halves[side] + swapped
    return total.astype(jnp.bfloat16)


def solution(mesh):
    return jax.shard_map(
        body,
        mesh=mesh,
        in_specs=(
            P("seq", "mp"),
            P(),
            P(),
            P(None, "mp"),
            P(None, None, "mp"),
            P("mp", None),
            P("seq", "mp"),
            P("seq", "mp"),
            P(),
            P(),
            P(),
        ),
        out_specs=P(("seq", "mp"), None),
        check_vma=False,
    )
```
